512 devices in a mesh: dp: 8 (over x, y_hi), seq: 64 (over z, y_lo, core).
Axes of the slice: x: 4, y: 8 (y_hi: 2, y_lo: 4; y = y_hi * 4 + y_lo), z: 8, core: 2. Of those that a mesh axis runs over, the one named last changes fastest.
Arguments:
- tokens: bfloat16 [8, 128, 256, 768], P('dp', 'seq'), may hold values from -6 to 6
- upstream: bfloat16 [8, 128, 256, 768], P('dp', 'seq'), may hold values from -0.078125 to 0.078125
- row_factor: bfloat16 [128, 256, 256], P('seq'), may hold values from -0.375 to 0.375
- column_factor: bfloat16 [256, 128, 128], P('seq'), may hold values from -0.5 to 0.5
Outputs:
- grad_row: bfloat16 [128, 256, 256], P('seq')
- grad_column: bfloat16 [256, 128, 128], P('seq')
The draws below stay inside these ranges and needn't reach their ends.
All inputs are finite; a program needn't handle non-finite values.
Results may differ from the reference program's by a relative error of at most 0.005.
Values may be sent and summed in bfloat16 or wider, within the bound.
No kernel may reach another device: no remote copies, remote signals or barrier semaphores. Data moves between devices by JAX's collectives and lax.ppermute only.
A program may use at most 64 MiB of HBM per device.

```python
import jax
import jax.numpy as jnp
from jax import lax

C = 256
D = 768
R = 128
DOCS = 8


def level_of(stream_key, dims, split, smallest, top_value):
    factor_of, own = 1.0, jax.random.fold_in(stream_key, 6)
    for dim, shards_of in split:
        heights = jnp.exp(jax.random.uniform(jax.random.fold_in(own, dim), (shards_of,), jnp.float32, smallest / len(split), top_value / len(split)))
        factor_of = factor_of * jnp.repeat(heights, dims[dim] // shards_of).reshape([-1 if axis == dim else 1 for axis in range(len(dims))])
    return factor_of


def bell_draw(stream_key, dims, deviation, limit, cuts=(), held_as=jnp.bfloat16):
    result = deviation * jax.random.normal(stream_key, dims, jnp.float32)
    if cuts:
        result = result * level_of(stream_key, dims, cuts, -0.22, 0.18)
    return jnp.clip(result, -limit, limit).astype(held_as)


def setup_inputs(seed: int = 0) -> dict:
    streams_of = jax.random.split(jax.random.key(seed), 5)
    return {
        "tokens": bell_draw(streams_of[0], (DOCS, R, C, D), 1.0, 6.0, ((0, 8), (1, 64))),
        "upstream": bell_draw(streams_of[1], (DOCS, R, C, D), (D * DOCS) ** -0.5, 0.078125, ((0, 8), (1, 64))),
        "row_factor": bell_draw(streams_of[2], (R, C, C), C ** -0.5, 0.375, ((0, 64),)),
        "column_factor": bell_draw(streams_of[3], (C, R, R), R ** -0.5, 0.5, ((0, 64),)),
    }


def reference(tokens, upstream, row_factor, column_factor):
    row_float = row_factor.astype(jnp.float32)
    column_float = column_factor.astype(jnp.float32)
    high = lax.Precision.HIGHEST

    def one_document(carry, pair):
        sum_row, sum_column = carry
        doc_tokens, doc_upstream = pair
        tokens_float = doc_tokens.astype(jnp.float32)
        upstream_float = doc_upstream.astype(jnp.float32)
        mixed = jnp.einsum("rij,rjd->rid", row_float, tokens_float, precision=high).astype(jnp.bfloat16)
        mixed_float = mixed.astype(jnp.float32)
        sum_column = sum_column + jnp.einsum("rcd,scd->crs", upstream_float, mixed_float, precision=high)
        back_mixed = jnp.einsum("crs,rcd->scd", column_float, upstream_float, precision=high).astype(jnp.bfloat16)
        sum_row = sum_row + jnp.einsum("rid,rjd->rij", back_mixed.astype(jnp.float32), tokens_float, precision=high)
        return (sum_row, sum_column), None

    start = (jnp.zeros(row_factor.shape, jnp.float32), jnp.zeros(column_factor.shape, jnp.float32))
    (sum_row, sum_column), unused = lax.scan(one_document, start, (tokens, upstream))
    return sum_row.astype(jnp.bfloat16), sum_column.astype(jnp.bfloat16)
```

```python
import jax
import jax.numpy as jnp
from jax import lax
from jax.sharding import PartitionSpec as P


def apply_rows(row_factor, tokens):
    return jnp.einsum(
        "rij,brjd->brid", row_factor, tokens, preferred_element_type=jnp.float32
    ).astype(jnp.bfloat16)


def reduce_docs(flat, n):
    mine = lax.all_to_all(flat.reshape(n, -1), "dp", 0, 0, tiled=True).sum(0)
    mine = mine.astype(jnp.bfloat16)
    spread = jnp.broadcast_to(mine[None], (n, mine.shape[0]))
    return lax.all_to_all(spread, "dp", 0, 0, tiled=True).reshape(-1)


def shards(tokens, upstream, row_factor, column_factor):
    n = lax.psum(1, "dp")
    k = lax.psum(1, "seq")
    _, rows, cols, d = tokens.shape
    mixed = apply_rows(row_factor, tokens)
    upstream_cols = lax.all_to_all(upstream, "seq", split_axis=2, concat_axis=1, tiled=True)
    back_cols = jnp.einsum(
        "crs,brcd->bscd", column_factor, upstream_cols, preferred_element_type=jnp.float32
    ).astype(jnp.bfloat16)
    ncol = cols // k
    send_m = mixed[0].reshape(rows, k, ncol, d).transpose(1, 0, 2, 3)
    send_b = back_cols[0].reshape(k, rows, ncol, d)
    got = lax.all_to_all(jnp.stack([send_m, send_b], 1), "seq", 0, 0, tiled=True)
    mixed_cols = got[:, 0].reshape(1, k * rows, ncol, d)
    back_rows = got[:, 1].transpose(1, 0, 2, 3).reshape(1, rows, cols, d)
    sum_column = jnp.einsum(
        "brcd,bscd->crs", upstream_cols, mixed_cols, preferred_element_type=jnp.float32
    )
    sum_row = jnp.einsum("brid,brjd->rij", back_rows, tokens, preferred_element_type=jnp.float32)
    flat = jnp.concatenate([sum_row.reshape(-1), sum_column.reshape(-1)])
    total = reduce_docs(flat, n)
    split = sum_row.size
    return (total[:split].reshape(sum_row.shape), total[split:].reshape(sum_column.shape))


def solution(mesh):
    placed = (
        P("dp", "seq", None, None),
        P("dp", "seq", None, None),
        P("seq", None, None),
        P("seq", None, None),
    )
    return jax.shard_map(
        shards,
        mesh=mesh,
        in_specs=placed,
        out_specs=(P("seq", None, None), P("seq", None, None)),
        check_vma=False,
    )
```

```python
import jax
import jax.numpy as jnp
from jax import lax
from jax.sharding import PartitionSpec as P


def apply_rows(row_factor, tokens):
    return jnp.einsum(
        "rij,brjd->brid", row_factor, tokens, preferred_element_type=jnp.float32
    ).astype(jnp.bfloat16)


def reduce_docs(sum_row, sum_column, n):
    rows = sum_row.reshape(n, -1, sum_row.shape[-1])
    cols = sum_column.reshape(n, -1, sum_row.shape[-1])
    flat = jnp.concatenate([rows, cols], axis=1)
    mine = lax.all_to_all(flat, "dp", 0, 0, tiled=True).sum(0).astype(jnp.bfloat16)
    spread = jnp.broadcast_to(mine[None], (n,) + mine.shape)
    total = lax.all_to_all(spread, "dp", 0, 0, tiled=True)
    split = rows.shape[1]
    return (total[:, :split].reshape(sum_row.shape), total[:, split:].reshape(sum_column.shape))


def shards(tokens, upstream, row_factor, column_factor):
    n = lax.psum(1, "dp")
    k = lax.psum(1, "seq")
    _, rows, cols, d = tokens.shape
    mixed = apply_rows(row_factor, tokens)
    upstream_cols = lax.all_to_all(upstream, "seq", split_axis=2, concat_axis=1, tiled=True)
    back_cols = jnp.einsum(
        "crs,brcd->bscd", column_factor, upstream_cols, preferred_element_type=jnp.float32
    ).astype(jnp.bfloat16)
    ncol = cols // k
    send_m = mixed[0].reshape(rows, k, ncol, d).transpose(1, 0, 2, 3)
    send_b = back_cols[0].reshape(k, rows, ncol, d)
    got = lax.all_to_all(jnp.stack([send_m, send_b], 1), "seq", 0, 0, tiled=True)
    mixed_cols = got[:, 0].reshape(1, k * rows, ncol, d)
    back_rows = got[:, 1].transpose(1, 0, 2, 3).reshape(1, rows, cols, d)
    sum_column = jnp.einsum(
        "brcd,bscd->crs", upstream_cols, mixed_cols, preferred_element_type=jnp.float32
    )
    sum_row = jnp.einsum("brid,brjd->rij", back_rows, tokens, preferred_element_type=jnp.float32)
    return reduce_docs(sum_row, sum_column, n)


def solution(mesh):
    placed = (
        P("dp", "seq", None, None),
        P("dp", "seq", None, None),
        P("seq", None, None),
        P("seq", None, None),
    )
    return jax.shard_map(
        shards,
        mesh=mesh,
        in_specs=placed,
        out_specs=(P("seq", None, None), P("seq", None, None)),
        check_vma=False,
    )
```

```python
import jax
import jax.numpy as jnp
from jax import lax
from jax.sharding import PartitionSpec as P

STAGES = (4, 2, 1)


def apply_rows(row_factor, tokens):
    return jnp.einsum(
        "rij,brjd->brid", row_factor, tokens, preferred_element_type=jnp.float32
    ).astype(jnp.bfloat16)


def halve_docs(part, n):
    q = lax.axis_index("dp")
    for bit in STAGES:
        half = part.shape[0] // 2
        mine = (q // bit) % 2
        keep = lax.dynamic_slice_in_dim(part, mine * half, half)
        give = lax.dynamic_slice_in_dim(part, (1 - mine) * half, half)
        part = keep + lax.ppermute(give, "dp", [(p, p ^ bit) for p in range(n)])
    return part


def shards(tokens, upstream, row_factor, column_factor):
    n = lax.psum(1, "dp")
    k = lax.psum(1, "seq")
    _, rows, cols, d = tokens.shape
    ncol = cols // k
    mixed = apply_rows(row_factor, tokens)
    send_u = upstream[0].reshape(rows, k, ncol, d).transpose(1, 0, 2, 3)
    send_m = mixed[0].reshape(rows, k, ncol, d).transpose(1, 0, 2, 3)
    got = lax.all_to_all(jnp.stack([send_u, send_m], 1), "seq", 0, 0, tiled=True)
    upstream_cols = got[:, 0].reshape(k * rows, ncol, d)
    mixed_cols = got[:, 1].reshape(k * rows, ncol, d)
    back_cols = jnp.einsum(
        "crs,rcd->scd", column_factor, upstream_cols, preferred_element_type=jnp.float32
    ).astype(jnp.bfloat16)
    back = lax.all_to_all(back_cols.reshape(k, rows, ncol, d), "seq", 0, 0, tiled=True)
    sum_column = jnp.einsum(
        "rcd,scd->crs", upstream_cols, mixed_cols, preferred_element_type=jnp.float32
    )
    width = cols
    col_part = halve_docs(sum_column.reshape(n, -1, width), n)
    col_part = col_part.astype(jnp.bfloat16).astype(jnp.float32)
    back_rows = back.transpose(1, 0, 2, 3).reshape(rows, cols, d)
    sum_row = jnp.einsum("rid,rjd->rij", back_rows, tokens[0], preferred_element_type=jnp.float32)
    row_parts = sum_row.reshape(n, -1, width)
    spread_col = jnp.broadcast_to(col_part, (n,) + col_part.shape[1:])
    got = lax.all_to_all(jnp.concatenate([row_parts, spread_col], 1), "dp", 0, 0, tiled=True)
    split = row_parts.shape[1]
    grad_column = got[:, split:].astype(jnp.bfloat16).reshape(sum_column.shape)
    row_mine = got[:, :split].sum(0).astype(jnp.bfloat16)
    total = lax.all_to_all(jnp.broadcast_to(row_mine[None], (n,) + row_mine.shape), "dp", 0, 0, tiled=True)
    return total.reshape(sum_row.shape), grad_column


def solution(mesh):
    placed = (
        P("dp", "seq", None, None),
        P("dp", "seq", None, None),
        P("seq", None, None),
        P("seq", None, None),
    )
    return jax.shard_map(
        shards,
        mesh=mesh,
        in_specs=placed,
        out_specs=(P("seq", None, None), P("seq", None, None)),
        check_vma=False,
    )
```
